32 devices in a mesh: dp: 4 (over y, core), decode: 8 (over z, x).
Axes of the slice: x: 2, y: 2, z: 4, core: 2. Of those that a mesh axis runs over, the one named last changes fastest.
Arguments:
- unique_ids: int32 [32768], P(('dp', 'decode')), may hold values from 0 to 5592404
- hash_mult: int32 [1024], replicated, may hold values from 1 to 32748
- hash_add: int32 [1024], replicated, may hold values from 0 to 32748
- lookups: int32 [16384, 26], P(('dp', 'decode')), may hold values from 0 to 1023
- weight_in: bfloat16 [1024, 1800], P(('dp', 'decode')), may hold values from -0.1875 to 0.1875
- bias_in: float32 [1800], replicated, may hold values from -3 to 3
- weight_out: bfloat16 [1800, 128], replicated, may hold values from -0.125 to 0.125
- bias_out: float32 [128], replicated, may hold values from -3 to 3
- cotangent: bfloat16 [16384, 3328], P(('dp', 'decode')), may hold values from -0.09375 to 0.09375
Outputs:
- sample_embeddings: bfloat16 [16384, 3328], P(('dp', 'decode'))
- grad_weight_in: float32 [1024, 1800], P(('dp', 'decode'))
- grad_bias_in: float32 [1800], replicated
- grad_weight_out: float32 [1800, 128], replicated
- grad_bias_out: float32 [128], replicated
The draws below stay inside these ranges and needn't reach their ends.
All inputs are finite; a program needn't handle non-finite values.
Results may differ from the reference program's by a relative error of at most 0.006.
Values may be sent and summed in bfloat16 or wider, within the bound.
No kernel may reach another device: no remote copies, remote signals or barrier semaphores. Data moves between devices by JAX's collectives and lax.ppermute only.
A program may use at most 128 MiB of HBM per device.

```python
import jax
import jax.numpy as jnp
from jax import lax

CODES = 1024
HIDDEN_SIZE = 1800
EMB = 128
FEATS = 26
BUCKETS = 32749
S_DEV = 512
U_DEV = 1024
SAMPLES = 16384
UNIQUE = 32768
N_DP = 4
N_DECODE = 8


def set_ends(values, key, least, high):
    longest = values.shape.index(max(values.shape))
    spots = []
    for shift in (0, 1):
        where = [jax.random.randint(jax.random.fold_in(key, axis), (), 0, length) for axis, length in enumerate(values.shape)]
        where[longest] = (where[longest] + shift) % values.shape[longest]
        spots.append(tuple(where))
    return values.at[spots[0]].set(least).at[spots[1]].set(high)


def block_scale(rng, extent, shards, smallest, largest):
    def one(dim, shards_of):
        heights = jax.random.uniform(jax.random.fold_in(jax.random.fold_in(rng, 6), dim), (shards_of,), jnp.float32, smallest / len(shards), largest / len(shards))
        return jnp.repeat(jnp.exp(heights), extent[dim] // shards_of).reshape((-1,) + (1,) * (len(extent) - dim - 1))

    level = one(*shards[0])
    for cut in shards[1:]:
        level = level * one(*cut)
    return level


def normal_values(key, extent, width, reach, pieces=(), held_as=jnp.bfloat16):
    level = block_scale(key, extent, pieces, -0.22, 0.18) if pieces else 1.0
    drawn = jax.random.normal(key, extent, jnp.float32) * width * level
    return jnp.minimum(jnp.maximum(drawn, -reach), reach).astype(held_as)


def setup_inputs(seed: int = 0) -> dict:
    key_of = jax.random.split(jax.random.key(seed), 10)
    unique_ids = set_ends(jax.random.randint(key_of[0], (UNIQUE,), 0, 5592405), jax.random.fold_in(key_of[0], 1), 0, 5592404).astype(jnp.int32)
    hash_mult = set_ends(jax.random.randint(key_of[1], (CODES,), 1, BUCKETS), jax.random.fold_in(key_of[1], 1), 1, BUCKETS - 1).astype(jnp.int32)
    hash_add = set_ends(jax.random.randint(key_of[2], (CODES,), 0, BUCKETS), jax.random.fold_in(key_of[2], 1), 0, BUCKETS - 1).astype(jnp.int32)
    lookups = set_ends(jax.random.randint(key_of[3], (SAMPLES, FEATS), 0, U_DEV), jax.random.fold_in(key_of[3], 1), 0, U_DEV - 1).astype(jnp.int32)
    weight_in = normal_values(key_of[4], (CODES, HIDDEN_SIZE), CODES ** -0.5, 0.1875, ((0, 32),))
    bias_in = normal_values(key_of[5], (HIDDEN_SIZE,), 0.5, 3.0, (), jnp.float32)
    weight_out = normal_values(key_of[6], (HIDDEN_SIZE, EMB), HIDDEN_SIZE ** -0.5, 0.125)
    bias_out = normal_values(key_of[7], (EMB,), 0.5, 3.0, (), jnp.float32)
    cotangent = normal_values(key_of[8], (SAMPLES, FEATS * EMB), (4.0 / (SAMPLES * FEATS) ** 0.5), 0.09375, ((0, 32),))
    return {"unique_ids": unique_ids, "hash_mult": hash_mult, "hash_add": hash_add, "lookups": lookups, "weight_in": weight_in, "bias_in": bias_in, "weight_out": weight_out, "bias_out": bias_out, "cotangent": cotangent}


def mish_act(values):
    return values * jnp.tanh(jax.nn.softplus(values))

def mish_backward(values, upstream):
    return jax.vjp(mish_act, values)[1](upstream)[0]

def encode_ids(id_values, hash_mult, hash_add):
    reduced = (id_values % BUCKETS).astype(jnp.int32)
    codes = ((hash_mult[None, :] * reduced[:, None] + hash_add[None, :]) % BUCKETS).astype(jnp.int32)
    code_scale = 2.0 / (BUCKETS - 1)
    return (codes.astype(jnp.float32) * code_scale - 1.0).astype(jnp.bfloat16)

def reference(unique_ids, hash_mult, hash_add, lookups, weight_in, bias_in, weight_out, bias_out, cotangent):
    blocks = N_DP * N_DECODE
    ids_blocked = unique_ids.reshape(blocks, U_DEV)
    lookups_blocked = lookups.reshape(blocks, S_DEV, FEATS)
    cot_blocked = cotangent.reshape(blocks, S_DEV, FEATS, EMB)

    def decode_block(totals, inputs):
        id_values, picked, upstream = inputs
        encoded = encode_ids(id_values, hash_mult, hash_add)
        pre_act = jnp.dot(encoded, weight_in, preferred_element_type=jnp.float32) + bias_in
        hidden = mish_act(pre_act).astype(jnp.bfloat16)
        embedded = (jnp.dot(hidden, weight_out, preferred_element_type=jnp.float32) + bias_out).astype(jnp.bfloat16)
        looked = jnp.take(embedded, picked.reshape(-1), axis=0).reshape(S_DEV, FEATS * EMB)
        one_hot = (picked[:, :, None] == jnp.arange(U_DEV, dtype=jnp.int32)[None, None, :]).astype(jnp.float32)
        d_embedded = jnp.einsum('sfu,sfe->ue', one_hot, upstream.astype(jnp.float32)).astype(jnp.bfloat16)
        d_hidden = jnp.dot(d_embedded, weight_out.T, preferred_element_type=jnp.float32)
        d_pre = mish_backward(pre_act, d_hidden).astype(jnp.bfloat16)
        sum_w_in, sum_b_in, sum_w_out, sum_b_out = totals
        sum_w_in = sum_w_in + jnp.dot(encoded.T, d_pre, preferred_element_type=jnp.float32)
        sum_b_in = sum_b_in + lax.optimization_barrier(jnp.sum(d_pre.astype(jnp.float32), axis=0))
        sum_w_out = sum_w_out + jnp.dot(hidden.T, d_embedded, preferred_element_type=jnp.float32)
        sum_b_out = sum_b_out + lax.optimization_barrier(jnp.sum(d_embedded.astype(jnp.float32), axis=0))
        return ((sum_w_in, sum_b_in, sum_w_out, sum_b_out), looked)
    initial = (jnp.zeros((CODES, HIDDEN_SIZE), jnp.float32), jnp.zeros((HIDDEN_SIZE,), jnp.float32), jnp.zeros((HIDDEN_SIZE, EMB), jnp.float32), jnp.zeros((EMB,), jnp.float32))
    totals, looked = lax.scan(decode_block, initial, (ids_blocked, lookups_blocked, cot_blocked))
    sum_w_in, sum_b_in, sum_w_out, sum_b_out = totals
    return (looked.reshape(SAMPLES, FEATS * EMB), sum_w_in, sum_b_in, sum_w_out, sum_b_out)
```

```python
import jax
import jax.numpy as jnp
from jax import lax
from jax.sharding import PartitionSpec as P

BUCKETS = 32749
AXES = ("dp", "decode")
CHUNK_ALIGN = 128
N_CHUNKS = 2


def mish_act(values):
    return values * jnp.tanh(jax.nn.softplus(values))


def mish_backward(values, upstream):
    return jax.vjp(mish_act, values)[1](upstream)[0]


def encode_ids(id_values, hash_mult, hash_add):
    reduced = id_values % BUCKETS
    codes = (hash_mult[None, :] * reduced[:, None] + hash_add[None, :]) % BUCKETS
    code_scale = 2.0 / (BUCKETS - 1)
    return (codes.astype(jnp.float32) * code_scale - 1.0).astype(jnp.bfloat16)


def chunk_bounds(width):
    step = -(-width // N_CHUNKS)
    step = -(-step // CHUNK_ALIGN) * CHUNK_ALIGN
    bounds = []
    start = 0
    while start < width:
        bounds.append((start, min(width, start + step)))
        start += step
    return bounds


def per_device(
    unique_ids, hash_mult, hash_add, lookups, weight_in, bias_in, weight_out, bias_out, cotangent
):
    unique_count = unique_ids.shape[0]
    sample_count = lookups.shape[0]
    feature_count = lookups.shape[1]
    code_count = hash_mult.shape[0]
    local_rows = weight_in.shape[0]
    hidden_width = weight_in.shape[1]
    embed_width = weight_out.shape[1]
    small_rows = embed_width + 2

    encoded = encode_ids(unique_ids, hash_mult, hash_add)

    upstream = cotangent.reshape(sample_count, feature_count, embed_width)
    half_count = feature_count // 2
    unique_index = jnp.arange(unique_count, dtype=jnp.int32)
    total = jnp.zeros((unique_count, embed_width), jnp.float32)
    for start_feature in (0, half_count):
        picked = lookups[:, start_feature : start_feature + half_count]
        one_hot = (picked[:, :, None] == unique_index[None, None, :]).astype(jnp.bfloat16)
        total = total + jnp.einsum(
            "sfu,sfe->ue",
            one_hot,
            upstream[:, start_feature : start_feature + half_count],
            preferred_element_type=jnp.float32,
        )
    d_rows = total.astype(jnp.bfloat16)
    local_b_out = jnp.sum(d_rows.astype(jnp.float32), axis=0)
    b_out_row = jnp.zeros((hidden_width,), jnp.float32).at[:embed_width].set(local_b_out)

    embedded_acc = jnp.zeros((unique_count, embed_width), jnp.float32)
    bounds = chunk_bounds(hidden_width)
    small_parts = []
    grad_parts = []
    for index, (lo, hi) in enumerate(bounds):
        w_in_c = lax.all_gather(weight_in[:, lo:hi], AXES, axis=0, tiled=True)
        pre_act = jnp.dot(encoded, w_in_c, preferred_element_type=jnp.float32) + bias_in[lo:hi]
        hidden = mish_act(pre_act).astype(jnp.bfloat16)
        w_out_c = weight_out[lo:hi]
        embedded_acc = embedded_acc + jnp.dot(hidden, w_out_c, preferred_element_type=jnp.float32)
        d_hidden = lax.dot_general(
            d_rows, w_out_c, (((1,), (1,)), ((), ())), preferred_element_type=jnp.float32
        )
        d_pre = mish_backward(pre_act, d_hidden).astype(jnp.bfloat16)
        g_w_in = lax.dot_general(
            encoded, d_pre, (((0,), (0,)), ((), ())), preferred_element_type=jnp.float32
        )
        g_w_out_t = lax.dot_general(
            d_rows, hidden, (((0,), (0,)), ((), ())), preferred_element_type=jnp.float32
        )
        g_b_in = jnp.sum(d_pre.astype(jnp.float32), axis=0)
        small = jnp.concatenate(
            [g_w_out_t, g_b_in[None, :], b_out_row[None, lo:hi]], axis=0
        ).reshape(-1)
        small_cols = -(-small.shape[0] // code_count)
        small = jnp.pad(small, (0, small_cols * code_count - small.shape[0]))
        combined = jnp.concatenate([g_w_in, small.reshape(code_count, small_cols)], axis=1)
        part = lax.psum_scatter(combined, AXES, scatter_dimension=0, tiled=True)
        grad_parts.append(part[:, : hi - lo])
        small_parts.append(part[:, hi - lo :])
    grad_w_in = jnp.concatenate(grad_parts, axis=1)
    small_all = lax.all_gather(jnp.concatenate(small_parts, axis=1), AXES, axis=0, tiled=True)
    pieces = []
    col = 0
    for lo, hi in bounds:
        cols = small_parts[len(pieces)].shape[1]
        flat = small_all[:, col : col + cols].reshape(-1)[: small_rows * (hi - lo)]
        pieces.append(flat.reshape(small_rows, hi - lo))
        col += cols
    small_all = jnp.concatenate(pieces, axis=1)
    grad_w_out = small_all[:embed_width].T
    grad_b_in = small_all[embed_width]
    grad_b_out = small_all[embed_width + 1, :embed_width]

    embedded = (embedded_acc + bias_out).astype(jnp.bfloat16)
    pick = (lookups[:, :, None] == unique_index[None, None, :]).astype(jnp.bfloat16)
    sample_out = (
        jnp.einsum("sfu,ue->sfe", pick, embedded, preferred_element_type=jnp.float32)
        .astype(jnp.bfloat16)
        .reshape(sample_count, feature_count * embed_width)
    )
    return (sample_out, grad_w_in, grad_b_in, grad_w_out, grad_b_out)


def solution(mesh):
    placed = (
        P(AXES),
        P(),
        P(),
        P(AXES, None),
        P(AXES, None),
        P(),
        P(),
        P(),
        P(AXES, None),
    )
    return jax.shard_map(
        per_device,
        mesh=mesh,
        in_specs=placed,
        out_specs=(P(AXES, None), P(AXES, None), P(), P(), P()),
        check_vma=False,
    )
```

```python
import jax
import jax.numpy as jnp
from jax import lax
from jax.sharding import PartitionSpec as P

BUCKETS = 32749
AXES = ("dp", "decode")
LANES = 128


def mish_act(values):
    return values * jnp.tanh(jax.nn.softplus(values))


def mish_backward(values, upstream):
    return jax.vjp(mish_act, values)[1](upstream)[0]


def encode_ids(id_values, hash_mult, hash_add):
    reduced = id_values % BUCKETS
    codes = (hash_mult[None, :] * reduced[:, None] + hash_add[None, :]) % BUCKETS
    code_scale = 2.0 / (BUCKETS - 1)
    return (codes.astype(jnp.float32) * code_scale - 1.0).astype(jnp.bfloat16)


def per_device(
    unique_ids, hash_mult, hash_add, lookups, weight_in, bias_in, weight_out, bias_out, cotangent
):
    unique_count = unique_ids.shape[0]
    sample_count = lookups.shape[0]
    feature_count = lookups.shape[1]
    code_count = hash_mult.shape[0]
    local_rows = weight_in.shape[0]
    hidden_width = weight_in.shape[1]
    embed_width = weight_out.shape[1]
    small_rows = embed_width + 2

    encoded = encode_ids(unique_ids, hash_mult, hash_add)

    upstream = cotangent.reshape(sample_count, feature_count, embed_width)
    half_count = feature_count // 2
    unique_index = jnp.arange(unique_count, dtype=jnp.int32)
    total = jnp.zeros((unique_count, embed_width), jnp.float32)
    for start_feature in (0, half_count):
        picked = lookups[:, start_feature : start_feature + half_count]
        one_hot = (picked[:, :, None] == unique_index[None, None, :]).astype(jnp.bfloat16)
        total = total + jnp.einsum(
            "sfu,sfe->ue",
            one_hot,
            upstream[:, start_feature : start_feature + half_count],
            preferred_element_type=jnp.float32,
        )
    d_rows = total.astype(jnp.bfloat16)
    local_b_out = jnp.sum(d_rows.astype(jnp.float32), axis=0)
    b_out_row = jnp.zeros((hidden_width,), jnp.float32).at[:embed_width].set(local_b_out)

    w_in_all = lax.all_gather(weight_in, AXES, axis=0, tiled=True)
    pre_act = jnp.dot(encoded, w_in_all, preferred_element_type=jnp.float32) + bias_in
    hidden = mish_act(pre_act).astype(jnp.bfloat16)
    embedded_acc = jnp.dot(hidden, weight_out, preferred_element_type=jnp.float32)
    d_hidden = lax.dot_general(
        d_rows, weight_out, (((1,), (1,)), ((), ())), preferred_element_type=jnp.float32
    )
    d_pre = mish_backward(pre_act, d_hidden).astype(jnp.bfloat16)
    g_w_in = lax.dot_general(
        encoded, d_pre, (((0,), (0,)), ((), ())), preferred_element_type=jnp.float32
    )
    g_w_out_t = lax.dot_general(
        d_rows, hidden, (((0,), (0,)), ((), ())), preferred_element_type=jnp.float32
    )
    g_b_in = jnp.sum(d_pre.astype(jnp.float32), axis=0)
    small = jnp.concatenate([g_w_out_t, g_b_in[None, :], b_out_row[None, :]], axis=0).reshape(-1)
    small_size = small.shape[0]
    total_cols = -(-(hidden_width + -(-small_size // code_count)) // LANES) * LANES
    small_cols = total_cols - hidden_width
    small = jnp.pad(small, (0, small_cols * code_count - small_size))
    combined = jnp.concatenate([g_w_in, small.reshape(code_count, small_cols)], axis=1)
    part = lax.psum_scatter(combined, AXES, scatter_dimension=0, tiled=True)
    grad_w_in = part[:, :hidden_width]
    gather_from = (hidden_width // LANES) * LANES
    small_all = lax.all_gather(part[:, gather_from:], AXES, axis=0, tiled=True)
    small_all = small_all[:, hidden_width - gather_from :].reshape(-1)[:small_size]
    small_all = small_all.reshape(small_rows, hidden_width)
    grad_w_out = small_all[:embed_width].T
    grad_b_in = small_all[embed_width]
    grad_b_out = small_all[embed_width + 1, :embed_width]

    embedded = (embedded_acc + bias_out).astype(jnp.bfloat16)
    pick = (lookups[:, :, None] == unique_index[None, None, :]).astype(jnp.bfloat16)
    sample_out = (
        jnp.einsum("sfu,ue->sfe", pick, embedded, preferred_element_type=jnp.float32)
        .astype(jnp.bfloat16)
        .reshape(sample_count, feature_count * embed_width)
    )
    return (sample_out, grad_w_in, grad_b_in, grad_w_out, grad_b_out)


def solution(mesh):
    placed = (
        P(AXES),
        P(),
        P(),
        P(AXES, None),
        P(AXES, None),
        P(),
        P(),
        P(),
        P(AXES, None),
    )
    return jax.shard_map(
        per_device,
        mesh=mesh,
        in_specs=placed,
        out_specs=(P(AXES, None), P(AXES, None), P(), P(), P()),
        check_vma=False,
    )
```

```python
import jax
import jax.numpy as jnp
from jax import lax
from jax.sharding import PartitionSpec as P

BUCKETS = 32749
AXES = ("dp", "decode")
LANES = 128


def mish_act(values):
    return values * jnp.tanh(jax.nn.softplus(values))


def mish_backward(values, upstream):
    return jax.vjp(mish_act, values)[1](upstream)[0]


def encode_ids(id_values, hash_mult, hash_add):
    reduced = id_values % BUCKETS
    codes = (hash_mult[None, :] * reduced[:, None] + hash_add[None, :]) % BUCKETS
    code_scale = 2.0 / (BUCKETS - 1)
    return (codes.astype(jnp.float32) * code_scale - 1.0).astype(jnp.bfloat16)


def gather_rows(values):
    for axis in reversed(AXES):
        values = lax.all_gather(values, axis, axis=0, tiled=True)
    return values


def scatter_rows(values):
    for axis in AXES:
        values = lax.psum_scatter(values, axis, scatter_dimension=0, tiled=True)
    return values


def per_device(
    unique_ids, hash_mult, hash_add, lookups, weight_in, bias_in, weight_out, bias_out, cotangent
):
    unique_count = unique_ids.shape[0]
    sample_count = lookups.shape[0]
    feature_count = lookups.shape[1]
    code_count = hash_mult.shape[0]
    local_rows = weight_in.shape[0]
    hidden_width = weight_in.shape[1]
    embed_width = weight_out.shape[1]
    small_rows = embed_width + 2

    encoded = encode_ids(unique_ids, hash_mult, hash_add)

    upstream = cotangent.reshape(sample_count, feature_count, embed_width)
    half_count = feature_count // 2
    unique_index = jnp.arange(unique_count, dtype=jnp.int32)
    total = jnp.zeros((unique_count, embed_width), jnp.float32)
    for start_feature in (0, half_count):
        picked = lookups[:, start_feature : start_feature + half_count]
        one_hot = (picked[:, :, None] == unique_index[None, None, :]).astype(jnp.bfloat16)
        total = total + jnp.einsum(
            "sfu,sfe->ue",
            one_hot,
            upstream[:, start_feature : start_feature + half_count],
            preferred_element_type=jnp.float32,
        )
    d_rows = total.astype(jnp.bfloat16)
    local_b_out = jnp.sum(d_rows.astype(jnp.float32), axis=0)
    b_out_row = jnp.zeros((hidden_width,), jnp.float32).at[:embed_width].set(local_b_out)

    w_in_all = gather_rows(weight_in)
    pre_act = jnp.dot(encoded, w_in_all, preferred_element_type=jnp.float32) + bias_in
    hidden = mish_act(pre_act).astype(jnp.bfloat16)
    embedded_acc = jnp.dot(hidden, weight_out, preferred_element_type=jnp.float32)
    d_hidden = lax.dot_general(
        d_rows, weight_out, (((1,), (1,)), ((), ())), preferred_element_type=jnp.float32
    )
    d_pre = mish_backward(pre_act, d_hidden).astype(jnp.bfloat16)
    g_w_in = lax.dot_general(
        encoded, d_pre, (((0,), (0,)), ((), ())), preferred_element_type=jnp.float32
    )
    g_w_out_t = lax.dot_general(
        d_rows, hidden, (((0,), (0,)), ((), ())), preferred_element_type=jnp.float32
    )
    g_b_in = jnp.sum(d_pre.astype(jnp.float32), axis=0)
    small = jnp.concatenate([g_w_out_t, g_b_in[None, :], b_out_row[None, :]], axis=0).reshape(-1)
    small_size = small.shape[0]
    total_cols = -(-(hidden_width + -(-small_size // code_count)) // LANES) * LANES
    small_cols = total_cols - hidden_width
    small = jnp.pad(small, (0, small_cols * code_count - small_size))
    combined = jnp.concatenate([g_w_in, small.reshape(code_count, small_cols)], axis=1)
    part = scatter_rows(combined)
    grad_w_in = part[:, :hidden_width]
    gather_from = (hidden_width // LANES) * LANES
    small_all = gather_rows(part[:, gather_from:])
    small_all = small_all[:, hidden_width - gather_from :].reshape(-1)[:small_size]
    small_all = small_all.reshape(small_rows, hidden_width)
    grad_w_out = small_all[:embed_width].T
    grad_b_in = small_all[embed_width]
    grad_b_out = small_all[embed_width + 1, :embed_width]

    embedded = (embedded_acc + bias_out).astype(jnp.bfloat16)
    pick = (lookups[:, :, None] == unique_index[None, None, :]).astype(jnp.bfloat16)
    sample_out = (
        jnp.einsum("sfu,ue->sfe", pick, embedded, preferred_element_type=jnp.float32)
        .astype(jnp.bfloat16)
        .reshape(sample_count, feature_count * embed_width)
    )
    return (sample_out, grad_w_in, grad_b_in, grad_w_out, grad_b_out)


def solution(mesh):
    placed = (
        P(AXES),
        P(),
        P(),
        P(AXES, None),
        P(AXES, None),
        P(),
        P(),
        P(),
        P(AXES, None),
    )
    return jax.shard_map(
        per_device,
        mesh=mesh,
        in_specs=placed,
        out_specs=(P(AXES, None), P(AXES, None), P(), P(), P()),
        check_vma=False,
    )
```

```python
import jax
import jax.numpy as jnp
from jax import lax
from jax.sharding import PartitionSpec as P

BUCKETS = 32749
AXES = ("dp", "decode")
LANES = 128


def mish_act(values):
    return values * jnp.tanh(jax.nn.softplus(values))


def mish_backward(values, upstream):
    return jax.vjp(mish_act, values)[1](upstream)[0]


def encode_ids(id_values, hash_mult, hash_add):
    reduced = id_values % BUCKETS
    codes = (hash_mult[None, :] * reduced[:, None] + hash_add[None, :]) % BUCKETS
    code_scale = 2.0 / (BUCKETS - 1)
    return (codes.astype(jnp.float32) * code_scale - 1.0).astype(jnp.bfloat16)


def gather_rows(values):
    for axis in reversed(AXES):
        values = lax.all_gather(values, axis, axis=0, tiled=True)
    return values


def scatter_rows(values):
    wide = values.dtype
    for index, axis in enumerate(AXES):
        sent = values.astype(jnp.bfloat16) if index == 0 else values
        values = lax.psum_scatter(sent, axis, scatter_dimension=0, tiled=True).astype(wide)
    return values


def per_device(
    unique_ids, hash_mult, hash_add, lookups, weight_in, bias_in, weight_out, bias_out, cotangent
):
    unique_count = unique_ids.shape[0]
    sample_count = lookups.shape[0]
    feature_count = lookups.shape[1]
    code_count = hash_mult.shape[0]
    local_rows = weight_in.shape[0]
    hidden_width = weight_in.shape[1]
    embed_width = weight_out.shape[1]
    small_rows = embed_width + 2

    encoded = encode_ids(unique_ids, hash_mult, hash_add)

    upstream = cotangent.reshape(sample_count, feature_count, embed_width)
    half_count = feature_count // 2
    unique_index = jnp.arange(unique_count, dtype=jnp.int32)
    total = jnp.zeros((unique_count, embed_width), jnp.float32)
    for start_feature in (0, half_count):
        picked = lookups[:, start_feature : start_feature + half_count]
        one_hot = (picked[:, :, None] == unique_index[None, None, :]).astype(jnp.bfloat16)
        total = total + jnp.einsum(
            "sfu,sfe->ue",
            one_hot,
            upstream[:, start_feature : start_feature + half_count],
            preferred_element_type=jnp.float32,
        )
    d_rows = total.astype(jnp.bfloat16)
    local_b_out = jnp.sum(d_rows.astype(jnp.float32), axis=0)
    b_out_row = jnp.zeros((hidden_width,), jnp.float32).at[:embed_width].set(local_b_out)

    w_in_all = gather_rows(weight_in)
    pre_act = jnp.dot(encoded, w_in_all, preferred_element_type=jnp.float32) + bias_in
    hidden = mish_act(pre_act).astype(jnp.bfloat16)
    embedded_acc = jnp.dot(hidden, weight_out, preferred_element_type=jnp.float32)
    d_hidden = lax.dot_general(
        d_rows, weight_out, (((1,), (1,)), ((), ())), preferred_element_type=jnp.float32
    )
    d_pre = mish_backward(pre_act, d_hidden).astype(jnp.bfloat16)
    g_w_in = lax.dot_general(
        encoded, d_pre, (((0,), (0,)), ((), ())), preferred_element_type=jnp.float32
    )
    g_w_out_t = lax.dot_general(
        d_rows, hidden, (((0,), (0,)), ((), ())), preferred_element_type=jnp.float32
    )
    g_b_in = jnp.sum(d_pre.astype(jnp.float32), axis=0)
    small = jnp.concatenate([g_w_out_t, g_b_in[None, :], b_out_row[None, :]], axis=0).reshape(-1)
    small_size = small.shape[0]
    total_cols = -(-(hidden_width + -(-small_size // code_count)) // LANES) * LANES
    small_cols = total_cols - hidden_width
    small = jnp.pad(small, (0, small_cols * code_count - small_size))
    combined = jnp.concatenate([g_w_in, small.reshape(code_count, small_cols)], axis=1)
    part = scatter_rows(combined)
    grad_w_in = part[:, :hidden_width]
    gather_from = (hidden_width // LANES) * LANES
    small_all = gather_rows(part[:, gather_from:])
    small_all = small_all[:, hidden_width - gather_from :].reshape(-1)[:small_size]
    small_all = small_all.reshape(small_rows, hidden_width)
    grad_w_out = small_all[:embed_width].T
    grad_b_in = small_all[embed_width]
    grad_b_out = small_all[embed_width + 1, :embed_width]

    embedded = (embedded_acc + bias_out).astype(jnp.bfloat16)
    pick = (lookups[:, :, None] == unique_index[None, None, :]).astype(jnp.bfloat16)
    sample_out = (
        jnp.einsum("sfu,ue->sfe", pick, embedded, preferred_element_type=jnp.float32)
        .astype(jnp.bfloat16)
        .reshape(sample_count, feature_count * embed_width)
    )
    return (sample_out, grad_w_in, grad_b_in, grad_w_out, grad_b_out)


def solution(mesh):
    placed = (
        P(AXES),
        P(),
        P(),
        P(AXES, None),
        P(AXES, None),
        P(),
        P(),
        P(),
        P(AXES, None),
    )
    return jax.shard_map(
        per_device,
        mesh=mesh,
        in_specs=placed,
        out_specs=(P(AXES, None), P(AXES, None), P(), P(), P()),
        check_vma=False,
    )
```

```python
import functools

import jax
import jax.numpy as jnp
from jax import lax
from jax.sharding import PartitionSpec as P

BUCKETS = 32749
AXES = ("dp", "decode")
LANES = 128


def mish_act(values):
    return values * jnp.tanh(jax.nn.softplus(values))


def mish_backward(values, upstream):
    return jax.vjp(mish_act, values)[1](upstream)[0]


def encode_ids(id_values, hash_mult, hash_add):
    reduced = id_values % BUCKETS
    codes = (hash_mult[None, :] * reduced[:, None] + hash_add[None, :]) % BUCKETS
    code_scale = 2.0 / (BUCKETS - 1)
    return (codes.astype(jnp.float32) * code_scale - 1.0).astype(jnp.bfloat16)


def shift_pairs(count, shift):
    return [(source, (source + shift) % count) for source in range(count)]


def gather_inner(values, count):
    where = lax.axis_index(AXES[1])
    received = [values]
    for shift in range(1, count):
        received.append(lax.ppermute(values, AXES[1], shift_pairs(count, shift)))
    stacked = jnp.stack(received)
    order = (where - jnp.arange(count, dtype=jnp.int32)) % count
    return jnp.take(stacked, order, axis=0).reshape((-1,) + values.shape[1:])


def scatter_inner(values, count):
    where = lax.axis_index(AXES[1])
    blocks = values.reshape((count, -1) + values.shape[1:])
    total = lax.dynamic_index_in_dim(blocks, where, axis=0, keepdims=False)
    for shift in range(1, count):
        sent = lax.dynamic_index_in_dim(blocks, (where + shift) % count, axis=0, keepdims=False)
        total = total + lax.ppermute(sent, AXES[1], shift_pairs(count, shift))
    return total


def gather_rows(values, count):
    values = gather_inner(values, count)
    return lax.all_gather(values, AXES[0], axis=0, tiled=True)


def scatter_rows(values, count):
    wide = values.dtype
    values = lax.psum_scatter(
        values.astype(jnp.bfloat16), AXES[0], scatter_dimension=0, tiled=True
    ).astype(wide)
    return scatter_inner(values, count)


def per_device(
    inner_count,
    unique_ids, hash_mult, hash_add, lookups, weight_in, bias_in, weight_out, bias_out, cotangent
):
    unique_count = unique_ids.shape[0]
    sample_count = lookups.shape[0]
    feature_count = lookups.shape[1]
    code_count = hash_mult.shape[0]
    local_rows = weight_in.shape[0]
    hidden_width = weight_in.shape[1]
    embed_width = weight_out.shape[1]
    small_rows = embed_width + 2

    encoded = encode_ids(unique_ids, hash_mult, hash_add)

    upstream = cotangent.reshape(sample_count, feature_count, embed_width)
    half_count = feature_count // 2
    unique_index = jnp.arange(unique_count, dtype=jnp.int32)
    total = jnp.zeros((unique_count, embed_width), jnp.float32)
    for start_feature in (0, half_count):
        picked = lookups[:, start_feature : start_feature + half_count]
        one_hot = (picked[:, :, None] == unique_index[None, None, :]).astype(jnp.bfloat16)
        total = total + jnp.einsum(
            "sfu,sfe->ue",
            one_hot,
            upstream[:, start_feature : start_feature + half_count],
            preferred_element_type=jnp.float32,
        )
    d_rows = total.astype(jnp.bfloat16)
    local_b_out = jnp.sum(d_rows.astype(jnp.float32), axis=0)
    b_out_row = jnp.zeros((hidden_width,), jnp.float32).at[:embed_width].set(local_b_out)

    w_in_all = gather_rows(weight_in, inner_count)
    pre_act = jnp.dot(encoded, w_in_all, preferred_element_type=jnp.float32) + bias_in
    hidden = mish_act(pre_act).astype(jnp.bfloat16)
    embedded_acc = jnp.dot(hidden, weight_out, preferred_element_type=jnp.float32)
    d_hidden = lax.dot_general(
        d_rows, weight_out, (((1,), (1,)), ((), ())), preferred_element_type=jnp.float32
    )
    d_pre = mish_backward(pre_act, d_hidden).astype(jnp.bfloat16)
    g_w_in = lax.dot_general(
        encoded, d_pre, (((0,), (0,)), ((), ())), preferred_element_type=jnp.float32
    )
    g_w_out_t = lax.dot_general(
        d_rows, hidden, (((0,), (0,)), ((), ())), preferred_element_type=jnp.float32
    )
    g_b_in = jnp.sum(d_pre.astype(jnp.float32), axis=0)
    small = jnp.concatenate([g_w_out_t, g_b_in[None, :], b_out_row[None, :]], axis=0).reshape(-1)
    small_size = small.shape[0]
    total_cols = -(-(hidden_width + -(-small_size // code_count)) // LANES) * LANES
    small_cols = total_cols - hidden_width
    small = jnp.pad(small, (0, small_cols * code_count - small_size))
    combined = jnp.concatenate([g_w_in, small.reshape(code_count, small_cols)], axis=1)
    part = scatter_rows(combined, inner_count)
    grad_w_in = part[:, :hidden_width]
    gather_from = (hidden_width // LANES) * LANES
    small_all = gather_rows(part[:, gather_from:], inner_count)
    small_all = small_all[:, hidden_width - gather_from :].reshape(-1)[:small_size]
    small_all = small_all.reshape(small_rows, hidden_width)
    grad_w_out = small_all[:embed_width].T
    grad_b_in = small_all[embed_width]
    grad_b_out = small_all[embed_width + 1, :embed_width]

    embedded = (embedded_acc + bias_out).astype(jnp.bfloat16)
    pick = (lookups[:, :, None] == unique_index[None, None, :]).astype(jnp.bfloat16)
    sample_out = (
        jnp.einsum("sfu,ue->sfe", pick, embedded, preferred_element_type=jnp.float32)
        .astype(jnp.bfloat16)
        .reshape(sample_count, feature_count * embed_width)
    )
    return (sample_out, grad_w_in, grad_b_in, grad_w_out, grad_b_out)


def solution(mesh):
    placed = (
        P(AXES),
        P(),
        P(),
        P(AXES, None),
        P(AXES, None),
        P(),
        P(),
        P(),
        P(AXES, None),
    )
    return jax.shard_map(
        functools.partial(per_device, mesh.shape[AXES[1]]),
        mesh=mesh,
        in_specs=placed,
        out_specs=(P(AXES, None), P(AXES, None), P(), P(), P()),
        check_vma=False,
    )
```

```python
import functools

import jax
import jax.numpy as jnp
from jax import lax
from jax.sharding import PartitionSpec as P

BUCKETS = 32749
AXES = ("dp", "decode")
LANES = 128


def mish_act(values):
    return values * jnp.tanh(jax.nn.softplus(values))


def mish_backward(values, upstream):
    return jax.vjp(mish_act, values)[1](upstream)[0]


def encode_ids(id_values, hash_mult, hash_add):
    reduced = id_values % BUCKETS
    codes = (hash_mult[None, :] * reduced[:, None] + hash_add[None, :]) % BUCKETS
    code_scale = 2.0 / (BUCKETS - 1)
    return (codes.astype(jnp.float32) * code_scale - 1.0).astype(jnp.bfloat16)


def shift_pairs(count, shift):
    return [(source, (source + shift) % count) for source in range(count)]


def gather_inner(values, count):
    where = lax.axis_index(AXES[1])
    received = [values]
    for shift in range(1, count):
        received.append(lax.ppermute(values, AXES[1], shift_pairs(count, shift)))
    stacked = jnp.stack(received)
    order = (where - jnp.arange(count, dtype=jnp.int32)) % count
    return jnp.take(stacked, order, axis=0).reshape((-1,) + values.shape[1:])


def scatter_inner(values, count):
    where = lax.axis_index(AXES[1])
    blocks = values.reshape((count, -1) + values.shape[1:])
    total = lax.dynamic_index_in_dim(blocks, where, axis=0, keepdims=False)
    for shift in range(1, count):
        sent = lax.dynamic_index_in_dim(blocks, (where + shift) % count, axis=0, keepdims=False)
        total = total + lax.ppermute(sent, AXES[1], shift_pairs(count, shift))
    return total


def gather_rows(values, count):
    values = gather_inner(values, count)
    return lax.all_gather(values, AXES[0], axis=0, tiled=True)


def scatter_rows(values, count, companion):
    wide = values.dtype
    values = lax.psum_scatter(
        values.astype(jnp.bfloat16), AXES[0], scatter_dimension=0, tiled=True
    )
    values, companion = lax.optimization_barrier((values, companion))
    return scatter_inner(values.astype(wide), count), companion


def per_device(
    inner_count,
    unique_ids, hash_mult, hash_add, lookups, weight_in, bias_in, weight_out, bias_out, cotangent
):
    unique_count = unique_ids.shape[0]
    sample_count = lookups.shape[0]
    feature_count = lookups.shape[1]
    code_count = hash_mult.shape[0]
    local_rows = weight_in.shape[0]
    hidden_width = weight_in.shape[1]
    embed_width = weight_out.shape[1]
    small_rows = embed_width + 2

    encoded = encode_ids(unique_ids, hash_mult, hash_add)

    upstream = cotangent.reshape(sample_count, feature_count, embed_width)
    half_count = feature_count // 2
    unique_index = jnp.arange(unique_count, dtype=jnp.int32)
    total = jnp.zeros((unique_count, embed_width), jnp.float32)
    for start_feature in (0, half_count):
        picked = lookups[:, start_feature : start_feature + half_count]
        one_hot = (picked[:, :, None] == unique_index[None, None, :]).astype(jnp.bfloat16)
        total = total + jnp.einsum(
            "sfu,sfe->ue",
            one_hot,
            upstream[:, start_feature : start_feature + half_count],
            preferred_element_type=jnp.float32,
        )
    d_rows = total.astype(jnp.bfloat16)
    local_b_out = jnp.sum(d_rows.astype(jnp.float32), axis=0)
    b_out_row = jnp.zeros((hidden_width,), jnp.float32).at[:embed_width].set(local_b_out)

    w_in_all = gather_rows(weight_in, inner_count)
    pre_act = jnp.dot(encoded, w_in_all, preferred_element_type=jnp.float32) + bias_in
    hidden = mish_act(pre_act).astype(jnp.bfloat16)
    embedded_acc = jnp.dot(hidden, weight_out, preferred_element_type=jnp.float32)
    d_hidden = lax.dot_general(
        d_rows, weight_out, (((1,), (1,)), ((), ())), preferred_element_type=jnp.float32
    )
    d_pre = mish_backward(pre_act, d_hidden).astype(jnp.bfloat16)
    g_w_in = lax.dot_general(
        encoded, d_pre, (((0,), (0,)), ((), ())), preferred_element_type=jnp.float32
    )
    g_w_out_t = lax.dot_general(
        d_rows, hidden, (((0,), (0,)), ((), ())), preferred_element_type=jnp.float32
    )
    g_b_in = jnp.sum(d_pre.astype(jnp.float32), axis=0)
    small = jnp.concatenate([g_w_out_t, g_b_in[None, :], b_out_row[None, :]], axis=0).reshape(-1)
    small_size = small.shape[0]
    total_cols = -(-(hidden_width + -(-small_size // code_count)) // LANES) * LANES
    small_cols = total_cols - hidden_width
    small = jnp.pad(small, (0, small_cols * code_count - small_size))
    combined = jnp.concatenate([g_w_in, small.reshape(code_count, small_cols)], axis=1)
    embedded = (embedded_acc + bias_out).astype(jnp.bfloat16)
    pick = (lookups[:, :, None] == unique_index[None, None, :]).astype(jnp.bfloat16)
    sample_out = (
        jnp.einsum("sfu,ue->sfe", pick, embedded, preferred_element_type=jnp.float32)
        .astype(jnp.bfloat16)
        .reshape(sample_count, feature_count * embed_width)
    )
    part, sample_out = scatter_rows(combined, inner_count, sample_out)
    grad_w_in = part[:, :hidden_width]
    gather_from = (hidden_width // LANES) * LANES
    small_all = gather_rows(part[:, gather_from:], inner_count)
    small_all = small_all[:, hidden_width - gather_from :].reshape(-1)[:small_size]
    small_all = small_all.reshape(small_rows, hidden_width)
    grad_w_out = small_all[:embed_width].T
    grad_b_in = small_all[embed_width]
    grad_b_out = small_all[embed_width + 1, :embed_width]

    return (sample_out, grad_w_in, grad_b_in, grad_w_out, grad_b_out)


def solution(mesh):
    placed = (
        P(AXES),
        P(),
        P(),
        P(AXES, None),
        P(AXES, None),
        P(),
        P(),
        P(),
        P(AXES, None),
    )
    return jax.shard_map(
        functools.partial(per_device, mesh.shape[AXES[1]]),
        mesh=mesh,
        in_specs=placed,
        out_specs=(P(AXES, None), P(AXES, None), P(), P(), P()),
        check_vma=False,
    )
```

```python
import functools

import jax
import jax.numpy as jnp
from jax import lax
from jax.sharding import PartitionSpec as P

BUCKETS = 32749
AXES = ("dp", "decode")
LANES = 128


def mish_act(values):
    return values * jnp.tanh(jax.nn.softplus(values))


def mish_backward(values, upstream):
    return jax.vjp(mish_act, values)[1](upstream)[0]


def encode_ids(id_values, hash_mult, hash_add):
    reduced = id_values % BUCKETS
    codes = (hash_mult[None, :] * reduced[:, None] + hash_add[None, :]) % BUCKETS
    code_scale = 2.0 / (BUCKETS - 1)
    return (codes.astype(jnp.float32) * code_scale - 1.0).astype(jnp.bfloat16)


def shift_pairs(count, shift):
    return [(source, (source + shift) % count) for source in range(count)]


def gather_inner(values, count):
    where = lax.axis_index(AXES[1])
    received = [values]
    for shift in range(1, count):
        received.append(lax.ppermute(values, AXES[1], shift_pairs(count, shift)))
    stacked = jnp.stack(received)
    order = (where - jnp.arange(count, dtype=jnp.int32)) % count
    return jnp.take(stacked, order, axis=0).reshape((-1,) + values.shape[1:])


def scatter_inner(values, count, wide):
    where = lax.axis_index(AXES[1])
    blocks = values.reshape((count, -1) + values.shape[1:])
    total = lax.dynamic_index_in_dim(blocks, where, axis=0, keepdims=False).astype(wide)
    for shift in range(1, count):
        sent = lax.dynamic_index_in_dim(blocks, (where + shift) % count, axis=0, keepdims=False)
        total = total + lax.ppermute(sent, AXES[1], shift_pairs(count, shift)).astype(wide)
    return total


def gather_rows(values, count):
    values = gather_inner(values, count)
    return lax.all_gather(values, AXES[0], axis=0, tiled=True)


def scatter_rows(values, count, companion):
    wide = values.dtype
    values = lax.psum_scatter(
        values.astype(jnp.bfloat16), AXES[0], scatter_dimension=0, tiled=True
    )
    values, companion = lax.optimization_barrier((values, companion))
    return scatter_inner(values, count, wide), companion


def per_device(
    inner_count,
    unique_ids, hash_mult, hash_add, lookups, weight_in, bias_in, weight_out, bias_out, cotangent
):
    unique_count = unique_ids.shape[0]
    sample_count = lookups.shape[0]
    feature_count = lookups.shape[1]
    code_count = hash_mult.shape[0]
    local_rows = weight_in.shape[0]
    hidden_width = weight_in.shape[1]
    embed_width = weight_out.shape[1]
    small_rows = embed_width + 2

    encoded = encode_ids(unique_ids, hash_mult, hash_add)

    upstream = cotangent.reshape(sample_count, feature_count, embed_width)
    half_count = feature_count // 2
    unique_index = jnp.arange(unique_count, dtype=jnp.int32)
    total = jnp.zeros((unique_count, embed_width), jnp.float32)
    for start_feature in (0, half_count):
        picked = lookups[:, start_feature : start_feature + half_count]
        one_hot = (picked[:, :, None] == unique_index[None, None, :]).astype(jnp.bfloat16)
        total = total + jnp.einsum(
            "sfu,sfe->ue",
            one_hot,
            upstream[:, start_feature : start_feature + half_count],
            preferred_element_type=jnp.float32,
        )
    d_rows = total.astype(jnp.bfloat16)
    local_b_out = jnp.sum(d_rows.astype(jnp.float32), axis=0)
    b_out_row = jnp.zeros((hidden_width,), jnp.float32).at[:embed_width].set(local_b_out)

    w_in_all = gather_rows(weight_in, inner_count)
    pre_act = jnp.dot(encoded, w_in_all, preferred_element_type=jnp.float32) + bias_in
    hidden = mish_act(pre_act).astype(jnp.bfloat16)
    embedded_acc = jnp.dot(hidden, weight_out, preferred_element_type=jnp.float32)
    d_hidden = lax.dot_general(
        d_rows, weight_out, (((1,), (1,)), ((), ())), preferred_element_type=jnp.float32
    )
    d_pre = mish_backward(pre_act, d_hidden).astype(jnp.bfloat16)
    g_w_in = lax.dot_general(
        encoded, d_pre, (((0,), (0,)), ((), ())), preferred_element_type=jnp.float32
    )
    g_w_out_t = lax.dot_general(
        d_rows, hidden, (((0,), (0,)), ((), ())), preferred_element_type=jnp.float32
    )
    g_b_in = jnp.sum(d_pre.astype(jnp.float32), axis=0)
    small = jnp.concatenate([g_w_out_t, g_b_in[None, :], b_out_row[None, :]], axis=0).reshape(-1)
    small_size = small.shape[0]
    total_cols = -(-(hidden_width + -(-small_size // code_count)) // LANES) * LANES
    small_cols = total_cols - hidden_width
    small = jnp.pad(small, (0, small_cols * code_count - small_size))
    combined = jnp.concatenate([g_w_in, small.reshape(code_count, small_cols)], axis=1)
    embedded = (embedded_acc + bias_out).astype(jnp.bfloat16)
    pick = (lookups[:, :, None] == unique_index[None, None, :]).astype(jnp.bfloat16)
    sample_out = (
        jnp.einsum("sfu,ue->sfe", pick, embedded, preferred_element_type=jnp.float32)
        .astype(jnp.bfloat16)
        .reshape(sample_count, feature_count * embed_width)
    )
    part, sample_out = scatter_rows(combined, inner_count, sample_out)
    grad_w_in = part[:, :hidden_width]
    gather_from = (hidden_width // LANES) * LANES
    small_all = gather_rows(part[:, gather_from:], inner_count)
    small_all = small_all[:, hidden_width - gather_from :].reshape(-1)[:small_size]
    small_all = small_all.reshape(small_rows, hidden_width)
    grad_w_out = small_all[:embed_width].T
    grad_b_in = small_all[embed_width]
    grad_b_out = small_all[embed_width + 1, :embed_width]

    return (sample_out, grad_w_in, grad_b_in, grad_w_out, grad_b_out)


def solution(mesh):
    placed = (
        P(AXES),
        P(),
        P(),
        P(AXES, None),
        P(AXES, None),
        P(),
        P(),
        P(),
        P(AXES, None),
    )
    return jax.shard_map(
        functools.partial(per_device, mesh.shape[AXES[1]]),
        mesh=mesh,
        in_specs=placed,
        out_specs=(P(AXES, None), P(AXES, None), P(), P(), P()),
        check_vma=False,
    )
```

```python
import functools

import jax
import jax.numpy as jnp
from jax import lax
from jax.sharding import PartitionSpec as P

BUCKETS = 32749
AXES = ("dp", "decode")
LANES = 128


MISH_CLAMP = 20.0


def mish_parts(values):
    grown = jnp.exp(jnp.minimum(values, MISH_CLAMP))
    square = grown * (grown + 2.0)
    inverse = 1.0 / (square + 2.0)
    return grown, square, inverse


def mish_act(values):
    grown, square, inverse = mish_parts(values)
    return values * (square * inverse)


def mish_backward(values, upstream):
    grown, square, inverse = mish_parts(values)
    slope = square * inverse + 4.0 * values * grown * (grown + 1.0) * inverse * inverse
    return upstream * slope


def encode_ids(id_values, hash_mult, hash_add):
    reduced = id_values % BUCKETS
    codes = (hash_mult[None, :] * reduced[:, None] + hash_add[None, :]) % BUCKETS
    code_scale = 2.0 / (BUCKETS - 1)
    return (codes.astype(jnp.float32) * code_scale - 1.0).astype(jnp.bfloat16)


def shift_pairs(count, shift):
    return [(source, (source + shift) % count) for source in range(count)]


def gather_inner(values, count):
    where = lax.axis_index(AXES[1])
    received = [values]
    for shift in range(1, count):
        received.append(lax.ppermute(values, AXES[1], shift_pairs(count, shift)))
    stacked = jnp.stack(received)
    order = (where - jnp.arange(count, dtype=jnp.int32)) % count
    return jnp.take(stacked, order, axis=0).reshape((-1,) + values.shape[1:])


def scatter_inner(values, count, wide):
    where = lax.axis_index(AXES[1])
    blocks = values.reshape((count, -1) + values.shape[1:])
    total = lax.dynamic_index_in_dim(blocks, where, axis=0, keepdims=False).astype(wide)
    for shift in range(1, count):
        sent = lax.dynamic_index_in_dim(blocks, (where + shift) % count, axis=0, keepdims=False)
        total = total + lax.ppermute(sent, AXES[1], shift_pairs(count, shift)).astype(wide)
    return total


def gather_rows(values, count):
    values = gather_inner(values, count)
    return lax.all_gather(values, AXES[0], axis=0, tiled=True)


def scatter_rows(values, count, companion):
    wide = values.dtype
    values = lax.psum_scatter(
        values.astype(jnp.bfloat16), AXES[0], scatter_dimension=0, tiled=True
    )
    values, companion = lax.optimization_barrier((values, companion))
    return scatter_inner(values, count, wide), companion


def per_device(
    inner_count,
    unique_ids, hash_mult, hash_add, lookups, weight_in, bias_in, weight_out, bias_out, cotangent
):
    unique_count = unique_ids.shape[0]
    sample_count = lookups.shape[0]
    feature_count = lookups.shape[1]
    code_count = hash_mult.shape[0]
    local_rows = weight_in.shape[0]
    hidden_width = weight_in.shape[1]
    embed_width = weight_out.shape[1]
    small_rows = embed_width + 2

    encoded = encode_ids(unique_ids, hash_mult, hash_add)

    upstream = cotangent.reshape(sample_count, feature_count, embed_width)
    half_count = feature_count // 2
    unique_index = jnp.arange(unique_count, dtype=jnp.int32)
    total = jnp.zeros((unique_count, embed_width), jnp.float32)
    for start_feature in (0, half_count):
        picked = lookups[:, start_feature : start_feature + half_count]
        one_hot = (picked[:, :, None] == unique_index[None, None, :]).astype(jnp.bfloat16)
        total = total + jnp.einsum(
            "sfu,sfe->ue",
            one_hot,
            upstream[:, start_feature : start_feature + half_count],
            preferred_element_type=jnp.float32,
        )
    d_rows = total.astype(jnp.bfloat16)
    local_b_out = jnp.sum(d_rows.astype(jnp.float32), axis=0)
    b_out_row = jnp.zeros((hidden_width,), jnp.float32).at[:embed_width].set(local_b_out)

    w_in_all = gather_rows(weight_in, inner_count)
    pre_act = jnp.dot(encoded, w_in_all, preferred_element_type=jnp.float32) + bias_in
    hidden = mish_act(pre_act).astype(jnp.bfloat16)
    embedded_acc = jnp.dot(hidden, weight_out, preferred_element_type=jnp.float32)
    d_hidden = lax.dot_general(
        d_rows, weight_out, (((1,), (1,)), ((), ())), preferred_element_type=jnp.float32
    )
    d_pre = mish_backward(pre_act, d_hidden).astype(jnp.bfloat16)
    g_w_in = lax.dot_general(
        encoded, d_pre, (((0,), (0,)), ((), ())), preferred_element_type=jnp.float32
    )
    g_w_out_t = lax.dot_general(
        d_rows, hidden, (((0,), (0,)), ((), ())), preferred_element_type=jnp.float32
    )
    g_b_in = jnp.sum(d_pre.astype(jnp.float32), axis=0)
    small = jnp.concatenate([g_w_out_t, g_b_in[None, :], b_out_row[None, :]], axis=0).reshape(-1)
    small_size = small.shape[0]
    total_cols = -(-(hidden_width + -(-small_size // code_count)) // LANES) * LANES
    small_cols = total_cols - hidden_width
    small = jnp.pad(small, (0, small_cols * code_count - small_size))
    combined = jnp.concatenate([g_w_in, small.reshape(code_count, small_cols)], axis=1)
    embedded = (embedded_acc + bias_out).astype(jnp.bfloat16)
    pick = (lookups[:, :, None] == unique_index[None, None, :]).astype(jnp.bfloat16)
    sample_out = (
        jnp.einsum("sfu,ue->sfe", pick, embedded, preferred_element_type=jnp.float32)
        .astype(jnp.bfloat16)
        .reshape(sample_count, feature_count * embed_width)
    )
    part, sample_out = scatter_rows(combined, inner_count, sample_out)
    grad_w_in = part[:, :hidden_width]
    gather_from = (hidden_width // LANES) * LANES
    small_all = gather_rows(part[:, gather_from:], inner_count)
    small_all = small_all[:, hidden_width - gather_from :].reshape(-1)[:small_size]
    small_all = small_all.reshape(small_rows, hidden_width)
    grad_w_out = small_all[:embed_width].T
    grad_b_in = small_all[embed_width]
    grad_b_out = small_all[embed_width + 1, :embed_width]

    return (sample_out, grad_w_in, grad_b_in, grad_w_out, grad_b_out)


def solution(mesh):
    placed = (
        P(AXES),
        P(),
        P(),
        P(AXES, None),
        P(AXES, None),
        P(),
        P(),
        P(),
        P(AXES, None),
    )
    return jax.shard_map(
        functools.partial(per_device, mesh.shape[AXES[1]]),
        mesh=mesh,
        in_specs=placed,
        out_specs=(P(AXES, None), P(AXES, None), P(), P(), P()),
        check_vma=False,
    )
```

```python
import functools

import jax
import jax.numpy as jnp
from jax import lax
from jax.sharding import PartitionSpec as P

BUCKETS = 32749
AXES = ("dp", "decode")
LANES = 128


MISH_CLAMP = 20.0


def mish_parts(values):
    grown = jnp.exp(jnp.minimum(values, MISH_CLAMP))
    square = grown * (grown + 2.0)
    inverse = 1.0 / (square + 2.0)
    return grown, square, inverse


def mish_act(values):
    grown, square, inverse = mish_parts(values)
    return values * (square * inverse)


def mish_backward(values, upstream):
    grown, square, inverse = mish_parts(values)
    slope = square * inverse + 4.0 * values * grown * (grown + 1.0) * inverse * inverse
    return upstream * slope


def encode_ids(id_values, hash_mult, hash_add):
    reduced = id_values % BUCKETS
    codes = (hash_mult[None, :] * reduced[:, None] + hash_add[None, :]) % BUCKETS
    code_scale = 2.0 / (BUCKETS - 1)
    return (codes.astype(jnp.float32) * code_scale - 1.0).astype(jnp.bfloat16)


def shift_pairs(count, shift):
    return [(source, (source + shift) % count) for source in range(count)]


def gather_inner(values, count):
    where = lax.axis_index(AXES[1])
    received = [values]
    for shift in range(1, count):
        received.append(lax.ppermute(values, AXES[1], shift_pairs(count, shift)))
    stacked = jnp.stack(received)
    order = (where - jnp.arange(count, dtype=jnp.int32)) % count
    return jnp.take(stacked, order, axis=0).reshape((-1,) + values.shape[1:])


def scatter_axis(values, axis, count, wide):
    where = lax.axis_index(axis)
    blocks = values.reshape((count, -1) + values.shape[1:])
    total = lax.dynamic_index_in_dim(blocks, where, axis=0, keepdims=False).astype(wide)
    for shift in range(1, count):
        sent = lax.dynamic_index_in_dim(blocks, (where + shift) % count, axis=0, keepdims=False)
        sent = sent.astype(jnp.bfloat16)
        total = total + lax.ppermute(sent, axis, shift_pairs(count, shift)).astype(wide)
    return total


def gather_rows(values, count):
    values = gather_inner(values, count)
    return lax.all_gather(values, AXES[0], axis=0, tiled=True)


def scatter_rows(values, counts, companion):
    wide = values.dtype
    values = scatter_axis(values, AXES[0], counts[0], wide)
    values, companion = lax.optimization_barrier((values, companion))
    return scatter_axis(values, AXES[1], counts[1], wide), companion


def per_device(
    outer_count,
    inner_count,
    unique_ids, hash_mult, hash_add, lookups, weight_in, bias_in, weight_out, bias_out, cotangent
):
    unique_count = unique_ids.shape[0]
    sample_count = lookups.shape[0]
    feature_count = lookups.shape[1]
    code_count = hash_mult.shape[0]
    local_rows = weight_in.shape[0]
    hidden_width = weight_in.shape[1]
    embed_width = weight_out.shape[1]
    small_rows = embed_width + 2

    encoded = encode_ids(unique_ids, hash_mult, hash_add)

    upstream = cotangent.reshape(sample_count, feature_count, embed_width)
    half_count = feature_count // 2
    unique_index = jnp.arange(unique_count, dtype=jnp.int32)
    total = jnp.zeros((unique_count, embed_width), jnp.float32)
    for start_feature in (0, half_count):
        picked = lookups[:, start_feature : start_feature + half_count]
        one_hot = (picked[:, :, None] == unique_index[None, None, :]).astype(jnp.bfloat16)
        total = total + jnp.einsum(
            "sfu,sfe->ue",
            one_hot,
            upstream[:, start_feature : start_feature + half_count],
            preferred_element_type=jnp.float32,
        )
    d_rows = total.astype(jnp.bfloat16)
    local_b_out = jnp.sum(d_rows.astype(jnp.float32), axis=0)
    b_out_row = jnp.zeros((hidden_width,), jnp.float32).at[:embed_width].set(local_b_out)

    w_in_all = gather_rows(weight_in, inner_count)
    pre_act = jnp.dot(encoded, w_in_all, preferred_element_type=jnp.float32) + bias_in
    hidden = mish_act(pre_act).astype(jnp.bfloat16)
    embedded_acc = jnp.dot(hidden, weight_out, preferred_element_type=jnp.float32)
    d_hidden = lax.dot_general(
        d_rows, weight_out, (((1,), (1,)), ((), ())), preferred_element_type=jnp.float32
    )
    d_pre = mish_backward(pre_act, d_hidden).astype(jnp.bfloat16)
    g_w_in = lax.dot_general(
        encoded, d_pre, (((0,), (0,)), ((), ())), preferred_element_type=jnp.float32
    )
    g_w_out_t = lax.dot_general(
        d_rows, hidden, (((0,), (0,)), ((), ())), preferred_element_type=jnp.float32
    )
    g_b_in = jnp.sum(d_pre.astype(jnp.float32), axis=0)
    small = jnp.concatenate([g_w_out_t, g_b_in[None, :], b_out_row[None, :]], axis=0).reshape(-1)
    small_size = small.shape[0]
    total_cols = -(-(hidden_width + -(-small_size // code_count)) // LANES) * LANES
    small_cols = total_cols - hidden_width
    small = jnp.pad(small, (0, small_cols * code_count - small_size))
    combined = jnp.concatenate([g_w_in, small.reshape(code_count, small_cols)], axis=1)
    embedded = (embedded_acc + bias_out).astype(jnp.bfloat16)
    pick = (lookups[:, :, None] == unique_index[None, None, :]).astype(jnp.bfloat16)
    sample_out = (
        jnp.einsum("sfu,ue->sfe", pick, embedded, preferred_element_type=jnp.float32)
        .astype(jnp.bfloat16)
        .reshape(sample_count, feature_count * embed_width)
    )
    part, sample_out = scatter_rows(combined, (outer_count, inner_count), sample_out)
    grad_w_in = part[:, :hidden_width]
    gather_from = (hidden_width // LANES) * LANES
    small_all = gather_rows(part[:, gather_from:], inner_count)
    small_all = small_all[:, hidden_width - gather_from :].reshape(-1)[:small_size]
    small_all = small_all.reshape(small_rows, hidden_width)
    grad_w_out = small_all[:embed_width].T
    grad_b_in = small_all[embed_width]
    grad_b_out = small_all[embed_width + 1, :embed_width]

    return (sample_out, grad_w_in, grad_b_in, grad_w_out, grad_b_out)


def solution(mesh):
    placed = (
        P(AXES),
        P(),
        P(),
        P(AXES, None),
        P(AXES, None),
        P(),
        P(),
        P(),
        P(AXES, None),
    )
    return jax.shard_map(
        functools.partial(per_device, mesh.shape[AXES[0]], mesh.shape[AXES[1]]),
        mesh=mesh,
        in_specs=placed,
        out_specs=(P(AXES, None), P(AXES, None), P(), P(), P()),
        check_vma=False,
    )
```

```python
import functools

import jax
import jax.numpy as jnp
from jax import lax
from jax.sharding import PartitionSpec as P

BUCKETS = 32749
AXES = ("dp", "decode")
LANES = 128


MISH_CLAMP = 20.0


def mish_parts(values):
    grown = jnp.exp(jnp.minimum(values, MISH_CLAMP))
    square = grown * (grown + 2.0)
    inverse = 1.0 / (square + 2.0)
    return grown, square, inverse


def mish_act(values):
    grown, square, inverse = mish_parts(values)
    return values * (square * inverse)


def mish_backward(values, upstream):
    grown, square, inverse = mish_parts(values)
    slope = square * inverse + 4.0 * values * grown * (grown + 1.0) * inverse * inverse
    return upstream * slope


def encode_ids(id_values, hash_mult, hash_add):
    reduced = id_values % BUCKETS
    codes = (hash_mult[None, :] * reduced[:, None] + hash_add[None, :]) % BUCKETS
    code_scale = 2.0 / (BUCKETS - 1)
    return (codes.astype(jnp.float32) * code_scale - 1.0).astype(jnp.bfloat16)


def shift_pairs(count, shift):
    return [(source, (source + shift) % count) for source in range(count)]


def gather_inner(values, count):
    where = lax.axis_index(AXES[1])
    received = [values]
    for shift in range(1, count):
        received.append(lax.ppermute(values, AXES[1], shift_pairs(count, shift)))
    stacked = jnp.stack(received)
    order = (where - jnp.arange(count, dtype=jnp.int32)) % count
    return jnp.take(stacked, order, axis=0).reshape((-1,) + values.shape[1:])


def scatter_inner(values, count, wide):
    where = lax.axis_index(AXES[1])
    blocks = values.reshape((count, -1) + values.shape[1:])
    total = lax.dynamic_index_in_dim(blocks, where, axis=0, keepdims=False).astype(wide)
    for shift in range(1, count):
        sent = lax.dynamic_index_in_dim(blocks, (where + shift) % count, axis=0, keepdims=False)
        total = total + lax.ppermute(sent, AXES[1], shift_pairs(count, shift)).astype(wide)
    return total


def gather_rows(values, count):
    values = gather_inner(values, count)
    return lax.all_gather(values, AXES[0], axis=0, tiled=True)


def scatter_rows(values, count, companion):
    wide = values.dtype
    values = lax.psum_scatter(
        values.astype(jnp.bfloat16), AXES[0], scatter_dimension=0, tiled=True
    )
    values, companion = lax.optimization_barrier((values, companion))
    return scatter_inner(values, count, wide), companion


def per_device(
    inner_count,
    unique_ids, hash_mult, hash_add, lookups, weight_in, bias_in, weight_out, bias_out, cotangent
):
    unique_count = unique_ids.shape[0]
    sample_count = lookups.shape[0]
    feature_count = lookups.shape[1]
    code_count = hash_mult.shape[0]
    local_rows = weight_in.shape[0]
    hidden_width = weight_in.shape[1]
    embed_width = weight_out.shape[1]
    small_rows = embed_width + 2

    encoded = encode_ids(unique_ids, hash_mult, hash_add)

    upstream = cotangent.reshape(sample_count, feature_count, embed_width)
    half_count = feature_count // 2
    unique_index = jnp.arange(unique_count, dtype=jnp.int32)
    total = jnp.zeros((unique_count, embed_width), jnp.float32)
    for start_feature in (0, half_count):
        picked = lookups[:, start_feature : start_feature + half_count]
        one_hot = (picked[:, :, None] == unique_index[None, None, :]).astype(jnp.bfloat16)
        total = total + jnp.einsum(
            "sfu,sfe->ue",
            one_hot,
            upstream[:, start_feature : start_feature + half_count],
            preferred_element_type=jnp.float32,
        )
    d_rows = total.astype(jnp.bfloat16)
    local_b_out = jnp.sum(d_rows.astype(jnp.float32), axis=0)
    b_out_row = jnp.zeros((hidden_width,), jnp.float32).at[:embed_width].set(local_b_out)

    w_in_all = gather_rows(weight_in, inner_count)
    pre_act = jnp.dot(encoded, w_in_all, preferred_element_type=jnp.float32) + bias_in
    hidden = mish_act(pre_act).astype(jnp.bfloat16)
    embedded_acc = jnp.dot(hidden, weight_out, preferred_element_type=jnp.float32)
    d_hidden = lax.dot_general(
        d_rows, weight_out, (((1,), (1,)), ((), ())), preferred_element_type=jnp.float32
    )
    d_pre = mish_backward(pre_act, d_hidden).astype(jnp.bfloat16)
    g_w_in = lax.dot_general(
        encoded, d_pre, (((0,), (0,)), ((), ())), preferred_element_type=jnp.float32
    )
    g_w_out_t = lax.dot_general(
        d_rows, hidden, (((0,), (0,)), ((), ())), preferred_element_type=jnp.float32
    )
    g_b_in = jnp.sum(d_pre.astype(jnp.float32), axis=0)
    small = jnp.concatenate([g_w_out_t, g_b_in[None, :], b_out_row[None, :]], axis=0).reshape(-1)
    small_size = small.shape[0]
    total_cols = -(-(hidden_width + -(-small_size // code_count)) // LANES) * LANES
    small_cols = total_cols - hidden_width
    small = jnp.pad(small, (0, small_cols * code_count - small_size))
    combined = jnp.concatenate([g_w_in, small.reshape(code_count, small_cols)], axis=1)
    embedded = (embedded_acc + bias_out).astype(jnp.bfloat16)
    pick = (lookups[:, :, None] == unique_index[None, None, :]).astype(jnp.bfloat16)
    sample_out = (
        jnp.einsum("sfu,ue->sfe", pick, embedded, preferred_element_type=jnp.float32)
        .astype(jnp.bfloat16)
        .reshape(sample_count, feature_count * embed_width)
    )
    part, sample_out = scatter_rows(combined, inner_count, sample_out)
    grad_w_in = part[:, :hidden_width]
    gather_from = (hidden_width // LANES) * LANES
    small_all = gather_rows(part[:, gather_from:].astype(jnp.bfloat16), inner_count)
    small_all = small_all.astype(jnp.float32)
    small_all = small_all[:, hidden_width - gather_from :].reshape(-1)[:small_size]
    small_all = small_all.reshape(small_rows, hidden_width)
    grad_w_out = small_all[:embed_width].T
    grad_b_in = small_all[embed_width]
    grad_b_out = small_all[embed_width + 1, :embed_width]

    return (sample_out, grad_w_in, grad_b_in, grad_w_out, grad_b_out)


def solution(mesh):
    placed = (
        P(AXES),
        P(),
        P(),
        P(AXES, None),
        P(AXES, None),
        P(),
        P(),
        P(),
        P(AXES, None),
    )
    return jax.shard_map(
        functools.partial(per_device, mesh.shape[AXES[1]]),
        mesh=mesh,
        in_specs=placed,
        out_specs=(P(AXES, None), P(AXES, None), P(), P(), P()),
        check_vma=False,
    )
```

```python
import functools

import jax
import jax.numpy as jnp
from jax import lax
from jax.sharding import PartitionSpec as P

BUCKETS = 32749
AXES = ("dp", "decode")
LANES = 128


MISH_CLAMP = 20.0


def mish_parts(values):
    grown = jnp.exp(jnp.minimum(values, MISH_CLAMP))
    square = grown * (grown + 2.0)
    inverse = 1.0 / (square + 2.0)
    return grown, square, inverse


def mish_act(values):
    grown, square, inverse = mish_parts(values)
    return values * (square * inverse)


def mish_backward(values, upstream):
    grown, square, inverse = mish_parts(values)
    slope = square * inverse + 4.0 * values * grown * (grown + 1.0) * inverse * inverse
    return upstream * slope


def encode_ids(id_values, hash_mult, hash_add):
    reduced = id_values % BUCKETS
    codes = (hash_mult[None, :] * reduced[:, None] + hash_add[None, :]) % BUCKETS
    code_scale = 2.0 / (BUCKETS - 1)
    return (codes.astype(jnp.float32) * code_scale - 1.0).astype(jnp.bfloat16)


def shift_pairs(count, shift):
    return [(source, (source + shift) % count) for source in range(count)]


def gather_inner(values, count):
    where = lax.axis_index(AXES[1])
    received = [values]
    for shift in range(1, count):
        received.append(lax.ppermute(values, AXES[1], shift_pairs(count, shift)))
    stacked = jnp.stack(received)
    order = (where - jnp.arange(count, dtype=jnp.int32)) % count
    return jnp.take(stacked, order, axis=0).reshape((-1,) + values.shape[1:])


def scatter_inner(values, count, wide):
    where = lax.axis_index(AXES[1])
    blocks = values.reshape((count, -1) + values.shape[1:])
    total = lax.dynamic_index_in_dim(blocks, where, axis=0, keepdims=False).astype(wide)
    for shift in range(1, count):
        sent = lax.dynamic_index_in_dim(blocks, (where + shift) % count, axis=0, keepdims=False)
        total = total + lax.ppermute(sent, AXES[1], shift_pairs(count, shift)).astype(wide)
    return total


def sum_inner(values, count, wide):
    total = values.astype(wide)
    for shift in range(1, count):
        total = total + lax.ppermute(values, AXES[1], shift_pairs(count, shift)).astype(wide)
    return total


def gather_rows(values, count):
    values = gather_inner(values, count)
    return lax.all_gather(values, AXES[0], axis=0, tiled=True)


def scatter_rows(values, count, companion, split):
    wide = values.dtype
    values = lax.psum_scatter(
        values.astype(jnp.bfloat16), AXES[0], scatter_dimension=0, tiled=True
    )
    values, companion = lax.optimization_barrier((values, companion))
    main = scatter_inner(values[:, :split], count, wide)
    rest = sum_inner(values[:, split:], count, wide)
    return main, rest, companion


def per_device(
    inner_count,
    unique_ids, hash_mult, hash_add, lookups, weight_in, bias_in, weight_out, bias_out, cotangent
):
    unique_count = unique_ids.shape[0]
    sample_count = lookups.shape[0]
    feature_count = lookups.shape[1]
    code_count = hash_mult.shape[0]
    local_rows = weight_in.shape[0]
    hidden_width = weight_in.shape[1]
    embed_width = weight_out.shape[1]
    small_rows = embed_width + 2

    encoded = encode_ids(unique_ids, hash_mult, hash_add)

    upstream = cotangent.reshape(sample_count, feature_count, embed_width)
    half_count = feature_count // 2
    unique_index = jnp.arange(unique_count, dtype=jnp.int32)
    total = jnp.zeros((unique_count, embed_width), jnp.float32)
    for start_feature in (0, half_count):
        picked = lookups[:, start_feature : start_feature + half_count]
        one_hot = (picked[:, :, None] == unique_index[None, None, :]).astype(jnp.bfloat16)
        total = total + jnp.einsum(
            "sfu,sfe->ue",
            one_hot,
            upstream[:, start_feature : start_feature + half_count],
            preferred_element_type=jnp.float32,
        )
    d_rows = total.astype(jnp.bfloat16)
    local_b_out = jnp.sum(d_rows.astype(jnp.float32), axis=0)
    b_out_row = jnp.zeros((hidden_width,), jnp.float32).at[:embed_width].set(local_b_out)

    w_in_all = gather_rows(weight_in, inner_count)
    pre_act = jnp.dot(encoded, w_in_all, preferred_element_type=jnp.float32) + bias_in
    hidden = mish_act(pre_act).astype(jnp.bfloat16)
    embedded_acc = jnp.dot(hidden, weight_out, preferred_element_type=jnp.float32)
    d_hidden = lax.dot_general(
        d_rows, weight_out, (((1,), (1,)), ((), ())), preferred_element_type=jnp.float32
    )
    d_pre = mish_backward(pre_act, d_hidden).astype(jnp.bfloat16)
    g_w_in = lax.dot_general(
        encoded, d_pre, (((0,), (0,)), ((), ())), preferred_element_type=jnp.float32
    )
    g_w_out_t = lax.dot_general(
        d_rows, hidden, (((0,), (0,)), ((), ())), preferred_element_type=jnp.float32
    )
    g_b_in = jnp.sum(d_pre.astype(jnp.float32), axis=0)
    small = jnp.concatenate([g_w_out_t, g_b_in[None, :], b_out_row[None, :]], axis=0).reshape(-1)
    small_size = small.shape[0]
    total_cols = -(-(hidden_width + -(-small_size // code_count)) // LANES) * LANES
    small_cols = total_cols - hidden_width
    small = jnp.pad(small, (0, small_cols * code_count - small_size))
    combined = jnp.concatenate([g_w_in, small.reshape(code_count, small_cols)], axis=1)
    embedded = (embedded_acc + bias_out).astype(jnp.bfloat16)
    pick = (lookups[:, :, None] == unique_index[None, None, :]).astype(jnp.bfloat16)
    sample_out = (
        jnp.einsum("sfu,ue->sfe", pick, embedded, preferred_element_type=jnp.float32)
        .astype(jnp.bfloat16)
        .reshape(sample_count, feature_count * embed_width)
    )
    gather_from = (hidden_width // LANES) * LANES
    main, rest, sample_out = scatter_rows(combined, inner_count, sample_out, gather_from)
    own_rows = lax.dynamic_slice_in_dim(
        rest, lax.axis_index(AXES[1]) * local_rows, local_rows, axis=0
    )
    grad_w_in = jnp.concatenate([main, own_rows[:, : hidden_width - gather_from]], axis=1)
    small_all = lax.all_gather(rest.astype(jnp.bfloat16), AXES[0], axis=0, tiled=True)
    small_all = small_all.astype(jnp.float32)
    small_all = small_all[:, hidden_width - gather_from :].reshape(-1)[:small_size]
    small_all = small_all.reshape(small_rows, hidden_width)
    grad_w_out = small_all[:embed_width].T
    grad_b_in = small_all[embed_width]
    grad_b_out = small_all[embed_width + 1, :embed_width]

    return (sample_out, grad_w_in, grad_b_in, grad_w_out, grad_b_out)


def solution(mesh):
    placed = (
        P(AXES),
        P(),
        P(),
        P(AXES, None),
        P(AXES, None),
        P(),
        P(),
        P(),
        P(AXES, None),
    )
    return jax.shard_map(
        functools.partial(per_device, mesh.shape[AXES[1]]),
        mesh=mesh,
        in_specs=placed,
        out_specs=(P(AXES, None), P(AXES, None), P(), P(), P()),
        check_vma=False,
    )
```

```python
import functools

import jax
import jax.numpy as jnp
from jax import lax
from jax.sharding import PartitionSpec as P

BUCKETS = 32749
AXES = ("dp", "decode")
LANES = 128


MISH_CLAMP = 20.0


def mish_parts(values):
    grown = jnp.exp(jnp.minimum(values, MISH_CLAMP))
    square = grown * (grown + 2.0)
    inverse = 1.0 / (square + 2.0)
    return grown, square, inverse


def mish_act(values):
    grown, square, inverse = mish_parts(values)
    return values * (square * inverse)


def mish_backward(values, upstream):
    grown, square, inverse = mish_parts(values)
    slope = square * inverse + 4.0 * values * grown * (grown + 1.0) * inverse * inverse
    return upstream * slope


def encode_ids(id_values, hash_mult, hash_add):
    reduced = id_values % BUCKETS
    codes = (hash_mult[None, :] * reduced[:, None] + hash_add[None, :]) % BUCKETS
    code_scale = 2.0 / (BUCKETS - 1)
    return (codes.astype(jnp.float32) * code_scale - 1.0).astype(jnp.bfloat16)


def shift_pairs(count, shift):
    return [(source, (source + shift) % count) for source in range(count)]


def gather_inner(values, count, axis=AXES[1]):
    where = lax.axis_index(axis)
    received = [values]
    for shift in range(1, count):
        received.append(lax.ppermute(values, axis, shift_pairs(count, shift)))
    stacked = jnp.stack(received)
    order = (where - jnp.arange(count, dtype=jnp.int32)) % count
    return jnp.take(stacked, order, axis=0).reshape((-1,) + values.shape[1:])


def scatter_inner(values, count, wide):
    where = lax.axis_index(AXES[1])
    blocks = values.reshape((count, -1) + values.shape[1:])
    total = lax.dynamic_index_in_dim(blocks, where, axis=0, keepdims=False).astype(wide)
    for shift in range(1, count):
        sent = lax.dynamic_index_in_dim(blocks, (where + shift) % count, axis=0, keepdims=False)
        total = total + lax.ppermute(sent, AXES[1], shift_pairs(count, shift)).astype(wide)
    return total


def gather_rows(values, count):
    values = gather_inner(values, count)
    return lax.all_gather(values, AXES[0], axis=0, tiled=True)


def scatter_rows(values, count, companion):
    wide = values.dtype
    values = lax.psum_scatter(
        values.astype(jnp.bfloat16), AXES[0], scatter_dimension=0, tiled=True
    )
    values, companion = lax.optimization_barrier((values, companion))
    return scatter_inner(values, count, wide), companion


def per_device(
    outer_count,
    inner_count,
    unique_ids, hash_mult, hash_add, lookups, weight_in, bias_in, weight_out, bias_out, cotangent
):
    unique_count = unique_ids.shape[0]
    sample_count = lookups.shape[0]
    feature_count = lookups.shape[1]
    code_count = hash_mult.shape[0]
    local_rows = weight_in.shape[0]
    hidden_width = weight_in.shape[1]
    embed_width = weight_out.shape[1]
    small_rows = embed_width + 2

    encoded = encode_ids(unique_ids, hash_mult, hash_add)

    upstream = cotangent.reshape(sample_count, feature_count, embed_width)
    half_count = feature_count // 2
    unique_index = jnp.arange(unique_count, dtype=jnp.int32)
    total = jnp.zeros((unique_count, embed_width), jnp.float32)
    for start_feature in (0, half_count):
        picked = lookups[:, start_feature : start_feature + half_count]
        one_hot = (picked[:, :, None] == unique_index[None, None, :]).astype(jnp.bfloat16)
        total = total + jnp.einsum(
            "sfu,sfe->ue",
            one_hot,
            upstream[:, start_feature : start_feature + half_count],
            preferred_element_type=jnp.float32,
        )
    d_rows = total.astype(jnp.bfloat16)
    local_b_out = jnp.sum(d_rows.astype(jnp.float32), axis=0)
    b_out_row = jnp.zeros((hidden_width,), jnp.float32).at[:embed_width].set(local_b_out)

    w_in_all = gather_rows(weight_in, inner_count)
    pre_act = jnp.dot(encoded, w_in_all, preferred_element_type=jnp.float32) + bias_in
    hidden = mish_act(pre_act).astype(jnp.bfloat16)
    embedded_acc = jnp.dot(hidden, weight_out, preferred_element_type=jnp.float32)
    d_hidden = lax.dot_general(
        d_rows, weight_out, (((1,), (1,)), ((), ())), preferred_element_type=jnp.float32
    )
    d_pre = mish_backward(pre_act, d_hidden).astype(jnp.bfloat16)
    g_w_in = lax.dot_general(
        encoded, d_pre, (((0,), (0,)), ((), ())), preferred_element_type=jnp.float32
    )
    g_w_out_t = lax.dot_general(
        d_rows, hidden, (((0,), (0,)), ((), ())), preferred_element_type=jnp.float32
    )
    g_b_in = jnp.sum(d_pre.astype(jnp.float32), axis=0)
    small = jnp.concatenate([g_w_out_t, g_b_in[None, :], b_out_row[None, :]], axis=0).reshape(-1)
    small_size = small.shape[0]
    total_cols = -(-(hidden_width + -(-small_size // code_count)) // LANES) * LANES
    small_cols = total_cols - hidden_width
    small = jnp.pad(small, (0, small_cols * code_count - small_size))
    combined = jnp.concatenate([g_w_in, small.reshape(code_count, small_cols)], axis=1)
    embedded = (embedded_acc + bias_out).astype(jnp.bfloat16)
    pick = (lookups[:, :, None] == unique_index[None, None, :]).astype(jnp.bfloat16)
    sample_out = (
        jnp.einsum("sfu,ue->sfe", pick, embedded, preferred_element_type=jnp.float32)
        .astype(jnp.bfloat16)
        .reshape(sample_count, feature_count * embed_width)
    )
    part, sample_out = scatter_rows(combined, inner_count, sample_out)
    grad_w_in = part[:, :hidden_width]
    gather_from = (hidden_width // LANES) * LANES
    small_all = gather_inner(part[:, gather_from:].astype(jnp.bfloat16), inner_count)
    small_all = gather_inner(small_all, outer_count, AXES[0])
    small_all = small_all.astype(jnp.float32)
    small_all = small_all[:, hidden_width - gather_from :].reshape(-1)[:small_size]
    small_all = small_all.reshape(small_rows, hidden_width)
    grad_w_out = small_all[:embed_width].T
    grad_b_in = small_all[embed_width]
    grad_b_out = small_all[embed_width + 1, :embed_width]

    return (sample_out, grad_w_in, grad_b_in, grad_w_out, grad_b_out)


def solution(mesh):
    placed = (
        P(AXES),
        P(),
        P(),
        P(AXES, None),
        P(AXES, None),
        P(),
        P(),
        P(),
        P(AXES, None),
    )
    return jax.shard_map(
        functools.partial(per_device, mesh.shape[AXES[0]], mesh.shape[AXES[1]]),
        mesh=mesh,
        in_specs=placed,
        out_specs=(P(AXES, None), P(AXES, None), P(), P(), P()),
        check_vma=False,
    )
```
